512 devices in a mesh: row: 32 (over y, x, core), col: 16 (over z).
Axes of the slice: x: 4, y: 4, z: 16, core: 2. Of those that a mesh axis runs over, the one named last changes fastest.
Arguments:
- queries: bfloat16 [512, 16, 1024], P('row', None, 'col'), may hold values from -30 to 30
- new_keys: bfloat16 [512, 1024], P('row', 'col'), may hold values from -6 to 6
- new_values: bfloat16 [512, 1024], P('row', 'col'), may hold values from -12 to 12
- cache_keys: bfloat16 [512, 128, 1024], P('row', None, 'col'), may hold values from -8 to 8
- cache_values: bfloat16 [512, 128, 1024], P('row', None, 'col'), may hold values from -12 to 12
- lengths: int32 [512], P('row'), may hold values from 64 to 128
- parents: int32 [512], P('row'), may hold values from 0 to 511, as said below
- residual: bfloat16 [512, 16, 1024], P('row', None, 'col'), may hold values from -20 to 20
- norm_gain: bfloat16 [16, 1024], P(None, 'col'), may hold values from 0.5 to 1.5
- vocab_weight: bfloat16 [16, 1024, 64128], P(None, 'col', 'row')
Outputs:
- logprobs: float32 [512, 64128], P('col', 'row')
The draws below stay inside these ranges and needn't reach their ends.
Inputs may be any that keep to these rules, and one draw needn't show every extreme that they name: Among the 16 child beams of one index of row, at most 2 have their parents on the beams of any single index of row, and exactly 2 do for some index.
All inputs are finite; a program needn't handle non-finite values.
Results may differ from the reference program's by a relative error of at most 0.0015.
Values may be sent and summed in bfloat16 or wider, within the bound.
No kernel may reach another device: no remote copies, remote signals or barrier semaphores. Data moves between devices by JAX's collectives and lax.ppermute only.
A program may use at most 64 MiB of HBM per device.

```python
import jax
import jax.numpy as jnp
from jax import lax

KV_HEADS = 8
HEAD_DIM = 128
GROUP = 16
D = 16384
VOCAB = 64128
BEAMS_DEV = 16
BEAMS = 512
CTX = 128
CAP = 2
N_ROW = 32


def draw_queries(key, part):
    key_a = jax.random.fold_in(jax.random.fold_in(key, 11), 0)
    kv_width = KV_HEADS * HEAD_DIM
    noise_part = jax.random.normal(key_a, (BEAMS, GROUP, kv_width), jnp.float32)
    return jnp.clip(noise_part, -6.0, 6.0).astype(jnp.bfloat16)


def draw_cache_keys(key, part):
    kv_width = KV_HEADS * HEAD_DIM
    noise_part = jnp.clip(jax.random.normal(jax.random.fold_in(key, 13), (BEAMS, CTX, kv_width), jnp.float32), -6.0, 6.0)
    return noise_part.astype(jnp.bfloat16)


def draw_residual(key, part):
    key_a, key_b, key_c = jax.random.split(jax.random.fold_in(key, 17), 3)
    kv_width = KV_HEADS * HEAD_DIM
    row_scale = 10.0 ** jax.random.uniform(key_a, (BEAMS, 1, 1), jnp.float32)
    rising = 0.5 * jnp.arange(kv_width, dtype=jnp.float32) / kv_width
    col_scale = 10.0 ** (rising[None, None, :] + 0.5 * jax.random.uniform(key_b, (1, GROUP, kv_width), jnp.float32))
    base_part = jnp.clip(jax.random.normal(key_c, (BEAMS, GROUP, kv_width), jnp.float32), -4.0, 4.0)
    return (0.05 * row_scale * col_scale * base_part).astype(jnp.bfloat16)


def draw_vocab_weight(key, part):
    kv_width = KV_HEADS * HEAD_DIM
    shape_full = (GROUP, kv_width, VOCAB)
    factor = 3.0 / D ** 0.5 * (0.9 + 0.25 * jnp.arange(VOCAB, dtype=jnp.float32) / VOCAB)
    key_a = jax.random.fold_in(key, 19)
    base_part = jnp.clip(jax.random.normal(key_a, shape_full, jnp.float32), -6.0, 6.0)
    return (base_part * factor[None, None, :]).astype(jnp.bfloat16)


def draw_parents(key, part):
    base_key = jax.random.fold_in(key, 23)
    pool_size = CAP * N_ROW

    def per_device(device_index):
        sub_key = jax.random.fold_in(base_key, device_index)
        key_a, key_b, key_c, key_d = jax.random.split(sub_key, 4)
        owners = jnp.arange(pool_size, dtype=jnp.int32) // CAP
        favour = jax.random.randint(key_a, (), 0, N_ROW)
        draw_ranks = jax.random.permutation(key_b, pool_size).astype(jnp.int32)
        draw_ranks = jnp.where(owners == favour, -1 - jnp.arange(pool_size, dtype=jnp.int32) % CAP, draw_ranks)
        chosen = jnp.argsort(draw_ranks, stable=True)[:BEAMS_DEV]
        shuffle = jax.random.permutation(key_c, BEAMS_DEV)
        sources = owners[chosen][shuffle]
        offsets = jax.random.randint(key_d, (BEAMS_DEV,), 0, BEAMS_DEV)
        return (sources * BEAMS_DEV + offsets).astype(jnp.int32)
    return jax.vmap(per_device)(jnp.arange(N_ROW, dtype=jnp.int32)).reshape(BEAMS).astype(jnp.int32)


def plant(result, key, low, high):
    index_at = [jax.random.randint(jax.random.fold_in(key, axis), (), 0, length) for axis, length in enumerate(result.shape)]
    longest = result.shape.index(max(result.shape))
    neighbour = index_at[:longest] + [(index_at[longest] + 1) % result.shape[longest]] + index_at[longest + 1:]
    return result.at[tuple(index_at)].set(low).at[tuple(neighbour)].set(high)


def shard_levels(key, dims, pieces, low, high):
    loudness, own = 1.0, jax.random.fold_in(key, 6)
    for axis_at, blocks in pieces:
        steps = jnp.exp(jax.random.uniform(jax.random.fold_in(own, axis_at), (blocks,), jnp.float32, low / len(pieces), high / len(pieces)))
        loudness = loudness * jnp.repeat(steps, dims[axis_at] // blocks).reshape([-1 if axis == axis_at else 1 for axis in range(len(dims))])
    return loudness


def bell_draw(own_key, dims, scale, most, cuts=(), held_as=jnp.bfloat16):
    values = jax.random.normal(own_key, dims, jnp.float32) * scale
    if len(cuts) > 0:
        values = shard_levels(own_key, dims, cuts, -0.22, 0.18) * values
    return jnp.clip(values, min=-most, max=most).astype(held_as)


def setup_inputs(seed: int = 0) -> dict:
    arg_keys = jax.random.split(jax.random.key(seed), 11)
    return {
        "queries": draw_queries(jax.random.fold_in(arg_keys[10], 71), 0),
        "new_keys": bell_draw(arg_keys[1], (BEAMS, KV_HEADS * HEAD_DIM), 1.0, 6.0, ((0, 32), (1, 16))),
        "new_values": bell_draw(arg_keys[2], (BEAMS, KV_HEADS * HEAD_DIM), 2.0, 12.0, ((0, 32), (1, 16))),
        "cache_keys": draw_cache_keys(jax.random.fold_in(arg_keys[10], 71), 0),
        "cache_values": bell_draw(arg_keys[4], (BEAMS, CTX, KV_HEADS * HEAD_DIM), 2.0, 12.0, ((0, 32), (2, 16))),
        "lengths": plant(jax.random.randint(arg_keys[5], (BEAMS,), CTX // 2, CTX + 1), jax.random.fold_in(arg_keys[5], 1), CTX // 2, CTX).astype(jnp.int32),
        "parents": draw_parents(jax.random.fold_in(arg_keys[10], 71), 0),
        "residual": draw_residual(jax.random.fold_in(arg_keys[10], 71), 0),
        "norm_gain": jnp.clip(1.0 + 0.1 * jax.random.normal(arg_keys[8], (GROUP, KV_HEADS * HEAD_DIM), jnp.float32), 0.5, 1.5).astype(jnp.bfloat16),
        "vocab_weight": draw_vocab_weight(jax.random.fold_in(arg_keys[10], 71), 0),
    }


def reference(queries, new_keys, new_values, cache_keys, cache_values, lengths, parents, residual, norm_gain, vocab_weight):
    scale_factor = HEAD_DIM ** (-0.5)
    kept_keys = jnp.take(cache_keys, parents, axis=0)
    kept_values = jnp.take(cache_values, parents, axis=0)
    live_rows = jnp.take(lengths, parents, axis=0)
    query_heads = queries.astype(jnp.float32).reshape(BEAMS, GROUP, KV_HEADS, HEAD_DIM)
    key_heads = kept_keys.astype(jnp.float32).reshape(BEAMS, CTX, KV_HEADS, HEAD_DIM)
    value_heads = kept_values.astype(jnp.float32).reshape(BEAMS, CTX, KV_HEADS, HEAD_DIM)
    fresh_keys = new_keys.astype(jnp.float32).reshape(BEAMS, KV_HEADS, HEAD_DIM)
    fresh_values = new_values.astype(jnp.float32).reshape(BEAMS, 1, KV_HEADS, HEAD_DIM)
    cached = jnp.einsum('bjge,btge->bjgt', query_heads, key_heads, precision=lax.Precision.HIGHEST) * scale_factor
    own_score = jnp.einsum('bjge,bge->bjg', query_heads, fresh_keys, precision=lax.Precision.HIGHEST) * scale_factor
    positions = jnp.arange(CTX, dtype=jnp.int32)[None, None, None, :]
    visible = positions < live_rows[:, None, None, None]
    peak_score = jnp.maximum(lax.optimization_barrier(jnp.max(jnp.where(visible, cached, -jnp.inf), axis=-1)), own_score)
    weight = jnp.where(visible, jnp.exp(cached - peak_score[..., None]), jnp.float32(0.0))
    weight_own = jnp.exp(own_score - peak_score)
    weight_sum = lax.optimization_barrier(jnp.sum(weight, axis=-1)) + weight_own
    rounded = lax.optimization_barrier(weight.astype(jnp.bfloat16)).astype(jnp.float32)
    rounded_own = lax.optimization_barrier(weight_own.astype(jnp.bfloat16)).astype(jnp.float32)
    summed = jnp.einsum('bjgt,btge->bjge', rounded, value_heads, precision=lax.Precision.HIGHEST)
    own_part = rounded_own[..., None] * fresh_values
    attended = ((summed + own_part) / weight_sum[..., None]).reshape(BEAMS, GROUP, KV_HEADS * HEAD_DIM).astype(jnp.bfloat16)
    stream = residual.astype(jnp.float32) + attended.astype(jnp.float32)
    scaling = lax.rsqrt(lax.optimization_barrier(jnp.sum(stream * stream, axis=(1, 2))) / D + 1e-05)
    normed = (stream * norm_gain.astype(jnp.float32)[None] * scaling[:, None, None]).astype(jnp.bfloat16)
    logits = jnp.dot(normed.reshape(BEAMS, D), vocab_weight.reshape(D, VOCAB), preferred_element_type=jnp.float32)
    totals = lax.optimization_barrier(jnp.sum(jnp.exp(logits), axis=1))
    return logits - jnp.log(totals)[:, None]
```

```python
import jax
import jax.numpy as jnp
from jax import lax
from jax.sharding import PartitionSpec as P

HEAD_DIM = 128
D = 16384


def from_partner(value, axis, distance):
    mask = 2**distance
    pairs = [(source, source ^ mask) for source in range(lax.axis_size(axis))]
    return lax.ppermute(value, axis, pairs)


def exchange_sum(value, axis):
    size = lax.axis_size(axis)
    distance = 1
    while distance < size:
        pairs = [(source, source ^ distance) for source in range(size)]
        value = value + lax.ppermute(value, axis, pairs)
        distance *= 2
    return value


def count_before(sources):
    entries = sources.shape[-1]
    earlier = jnp.arange(entries)[:, None] > jnp.arange(entries)[None, :]
    matching = sources[..., :, None] == sources[..., None, :]
    return jnp.sum(matching & earlier, axis=-1)


def attend(queries_in, key_cache, value_cache, key_new, value_new, live_rows):
    leading = queries_in.shape[:-2]
    group_size = queries_in.shape[-2]
    panel_width = queries_in.shape[-1]
    head_part = min(panel_width, HEAD_DIM)
    heads_here = panel_width // head_part
    context = key_cache.shape[-2]
    query_heads = queries_in.reshape(leading + (group_size, heads_here, head_part))
    key_heads = key_cache.reshape(leading + (context, heads_here, head_part))
    value_heads = value_cache.reshape(leading + (context, heads_here, head_part))
    fresh_key = key_new.reshape(leading + (heads_here, head_part))
    fresh_value = value_new.reshape(leading + (1, heads_here, head_part)).astype(jnp.float32)
    cached = jnp.einsum(
        "...jhe,...the->...jht", query_heads, key_heads, preferred_element_type=jnp.float32
    )
    own_score = jnp.einsum(
        "...jhe,...he->...jh", query_heads, fresh_key, preferred_element_type=jnp.float32
    )
    other_cached, other_own = from_partner((cached, own_score), "col", 0)
    cached = cached + other_cached
    own_score = own_score + other_own
    scale_factor = HEAD_DIM ** (-0.5)
    cached = cached * scale_factor
    own_score = own_score * scale_factor
    positions = lax.broadcasted_iota(jnp.int32, cached.shape, cached.ndim - 1)
    visible = positions < live_rows.reshape(leading + (1, 1, 1))
    peak_score = jnp.maximum(jnp.max(jnp.where(visible, cached, -jnp.inf), axis=-1), own_score)
    weight = jnp.where(visible, jnp.exp(cached - peak_score[..., None]), jnp.float32(0.0))
    weight_own = jnp.exp(own_score - peak_score)
    weight_sum = jnp.sum(weight, axis=-1) + weight_own
    rounded = weight.astype(jnp.bfloat16)
    rounded_own = lax.optimization_barrier(weight_own.astype(jnp.bfloat16)).astype(jnp.float32)
    summed = jnp.einsum(
        "...jht,...the->...jhe", rounded, value_heads, preferred_element_type=jnp.float32
    )
    own_part = rounded_own[..., None] * fresh_value
    result = (summed + own_part) / weight_sum[..., None]
    return result.reshape(leading + (group_size, panel_width)).astype(jnp.bfloat16)


def body(
    queries,
    new_keys,
    new_values,
    cache_keys,
    cache_values,
    lengths,
    parents,
    residual,
    norm_gain,
    vocab_weight,
):
    row_count = lax.axis_size("row")
    beam_count = parents.shape[0]
    slot_cap = max(2, (2 * beam_count + row_count - 1) // row_count)
    my_row = lax.axis_index("row")
    group_size = queries.shape[1]
    panel_width = queries.shape[2]
    source = parents // beam_count
    rank_in = count_before(source)
    slot_index = source * slot_cap + rank_in
    slot_range = jnp.arange(slot_cap, dtype=jnp.int32)
    all_parents, all_lengths = (
        lax.all_gather(parents, "row", axis=0, tiled=True),
        lax.all_gather(lengths, "row", axis=0, tiled=True),
    )
    parent_table = all_parents.reshape(row_count, beam_count)
    sources_all = parent_table // beam_count
    offsets_all = parent_table % beam_count
    ranks_all = count_before(sources_all)
    chosen = (sources_all[:, None, :] == my_row) & (
        ranks_all[:, None, :] == slot_range[None, :, None]
    )
    rows_sent = jnp.sum(jnp.where(chosen, offsets_all[:, None, :], 0), axis=2)
    got_keys, got_values = (
        lax.all_to_all(cache_keys[rows_sent], "row", split_axis=0, concat_axis=0, tiled=True),
        lax.all_to_all(cache_values[rows_sent], "row", split_axis=0, concat_axis=0, tiled=True),
    )
    context = cache_keys.shape[1]
    kept_keys = got_keys.reshape(row_count * slot_cap, context, panel_width)[slot_index]
    kept_values = got_values.reshape(row_count * slot_cap, context, panel_width)[slot_index]
    attended = attend(queries, kept_keys, kept_values, new_keys, new_values, all_lengths[parents])
    stream = residual.astype(jnp.float32) + attended.astype(jnp.float32)
    square_sums = exchange_sum(jnp.sum(stream * stream, axis=(1, 2)), "col")
    scaling = lax.rsqrt(square_sums / D + 1e-05)
    normed = (stream * norm_gain.astype(jnp.float32)[None] * scaling[:, None, None]).astype(
        jnp.bfloat16
    )
    gathered = lax.all_gather(normed, "row", axis=0, tiled=True)
    flat_rows = gathered.reshape(gathered.shape[0], group_size * panel_width)
    flat_weight = vocab_weight.reshape(group_size * panel_width, vocab_weight.shape[2])
    logits = lax.psum_scatter(
        jnp.dot(flat_rows, flat_weight, preferred_element_type=jnp.float32),
        "col",
        scatter_dimension=0,
        tiled=True,
    )
    totals = exchange_sum(jnp.sum(jnp.exp(logits), axis=1), "row")
    return logits - jnp.log(totals)[:, None]


def solution(mesh):
    placed = (
        P("row", None, "col"),
        P("row", "col"),
        P("row", "col"),
        P("row", None, "col"),
        P("row", None, "col"),
        P("row"),
        P("row"),
        P("row", None, "col"),
        P(None, "col"),
        P(None, "col", "row"),
    )
    return jax.shard_map(
        body, mesh=mesh, in_specs=placed, out_specs=P("col", "row"), check_vma=False
    )
```

```python
import jax
import jax.numpy as jnp
from jax import lax
from jax.sharding import PartitionSpec as P

HEAD_DIM = 128
D = 16384


def from_partner(value, axis, distance):
    mask = 2**distance
    pairs = [(source, source ^ mask) for source in range(lax.axis_size(axis))]
    return lax.ppermute(value, axis, pairs)


def gather_from_all(value, axis):
    size = lax.axis_size(axis)
    copies = jnp.broadcast_to(value[None], (size,) + value.shape)
    got = lax.all_to_all(copies, axis, 0, 0, tiled=True)
    return got.reshape((size * value.shape[0],) + value.shape[1:])


def split_three(value):
    high = value.astype(jnp.bfloat16)
    rest = value - high.astype(jnp.float32)
    middle = rest.astype(jnp.bfloat16)
    low = (rest - middle.astype(jnp.float32)).astype(jnp.bfloat16)
    return jnp.stack([high, middle, low], axis=-1)


def count_before(sources):
    entries = sources.shape[-1]
    earlier = jnp.arange(entries)[:, None] > jnp.arange(entries)[None, :]
    matching = sources[..., :, None] == sources[..., None, :]
    return jnp.sum(matching & earlier, axis=-1)


def attend(queries_in, key_cache, value_cache, key_new, value_new, live_rows):
    leading = queries_in.shape[:-2]
    group_size = queries_in.shape[-2]
    panel_width = queries_in.shape[-1]
    head_part = min(panel_width, HEAD_DIM)
    heads_here = panel_width // head_part
    context = key_cache.shape[-2]
    query_heads = queries_in.reshape(leading + (group_size, heads_here, head_part))
    key_heads = key_cache.reshape(leading + (context, heads_here, head_part))
    value_heads = value_cache.reshape(leading + (context, heads_here, head_part))
    fresh_key = key_new.reshape(leading + (heads_here, head_part))
    fresh_value = value_new.reshape(leading + (1, heads_here, head_part)).astype(jnp.float32)
    cached = jnp.einsum(
        "...jhe,...the->...jht", query_heads, key_heads, preferred_element_type=jnp.float32
    )
    own_score = jnp.einsum(
        "...jhe,...he->...jh", query_heads, fresh_key, preferred_element_type=jnp.float32
    )
    other_cached, other_own = from_partner((cached, own_score), "col", 0)
    cached = cached + other_cached
    own_score = own_score + other_own
    scale_factor = HEAD_DIM ** (-0.5)
    cached = cached * scale_factor
    own_score = own_score * scale_factor
    positions = lax.broadcasted_iota(jnp.int32, cached.shape, cached.ndim - 1)
    visible = positions < live_rows.reshape(leading + (1, 1, 1))
    peak_score = jnp.maximum(jnp.max(jnp.where(visible, cached, -jnp.inf), axis=-1), own_score)
    weight = jnp.where(visible, jnp.exp(cached - peak_score[..., None]), jnp.float32(0.0))
    weight_own = jnp.exp(own_score - peak_score)
    weight_sum = jnp.sum(weight, axis=-1) + weight_own
    rounded = weight.astype(jnp.bfloat16)
    rounded_own = lax.optimization_barrier(weight_own.astype(jnp.bfloat16)).astype(jnp.float32)
    summed = jnp.einsum(
        "...jht,...the->...jhe", rounded, value_heads, preferred_element_type=jnp.float32
    )
    own_part = rounded_own[..., None] * fresh_value
    result = (summed + own_part) / weight_sum[..., None]
    return result.reshape(leading + (group_size, panel_width)).astype(jnp.bfloat16)


def body(
    queries,
    new_keys,
    new_values,
    cache_keys,
    cache_values,
    lengths,
    parents,
    residual,
    norm_gain,
    vocab_weight,
):
    row_count = lax.axis_size("row")
    beam_count = parents.shape[0]
    slot_cap = max(2, (2 * beam_count + row_count - 1) // row_count)
    my_row = lax.axis_index("row")
    group_size = queries.shape[1]
    panel_width = queries.shape[2]
    source = parents // beam_count
    rank_in = count_before(source)
    slot_index = source * slot_cap + rank_in
    slot_range = jnp.arange(slot_cap, dtype=jnp.int32)
    id_table = gather_from_all(jnp.stack([parents, lengths])[None], "row")
    all_parents = id_table[:, 0].reshape(-1)
    all_lengths = id_table[:, 1].reshape(-1)
    parent_table = all_parents.reshape(row_count, beam_count)
    sources_all = parent_table // beam_count
    offsets_all = parent_table % beam_count
    ranks_all = count_before(sources_all)
    chosen = (sources_all[:, None, :] == my_row) & (
        ranks_all[:, None, :] == slot_range[None, :, None]
    )
    rows_sent = jnp.sum(jnp.where(chosen, offsets_all[:, None, :], 0), axis=2)
    got_keys, got_values = (
        lax.all_to_all(cache_keys[rows_sent], "row", split_axis=0, concat_axis=0, tiled=True),
        lax.all_to_all(cache_values[rows_sent], "row", split_axis=0, concat_axis=0, tiled=True),
    )
    context = cache_keys.shape[1]
    kept_keys = got_keys.reshape(row_count * slot_cap, context, panel_width)[slot_index]
    kept_values = got_values.reshape(row_count * slot_cap, context, panel_width)[slot_index]
    attended = attend(queries, kept_keys, kept_values, new_keys, new_values, all_lengths[parents])
    stream = residual.astype(jnp.float32) + attended.astype(jnp.float32)
    square_part = jnp.sum(stream * stream, axis=(1, 2))
    unscaled = (stream * norm_gain.astype(jnp.float32)[None]).astype(jnp.bfloat16)
    pieces = split_three(square_part)
    extra = jnp.zeros((beam_count, 1, panel_width), jnp.bfloat16).at[:, 0, :3].set(pieces)
    gathered = gather_from_all(jnp.concatenate([unscaled, extra], axis=1), "row")
    flat_rows = gathered[:, :group_size, :].reshape(gathered.shape[0], group_size * panel_width)
    square_all = jnp.sum(gathered[:, group_size, :3].astype(jnp.float32), axis=1)
    flat_weight = vocab_weight.reshape(group_size * panel_width, vocab_weight.shape[2])
    partial = jnp.dot(flat_rows, flat_weight, preferred_element_type=jnp.float32)
    reduced = lax.psum_scatter(
        jnp.concatenate([partial, square_all[:, None]], axis=1),
        "col",
        scatter_dimension=0,
        tiled=True,
    )
    vocab_here = vocab_weight.shape[2]
    scaling = lax.rsqrt(reduced[:, vocab_here] / D + 1e-05)
    logits = reduced[:, :vocab_here] * scaling[:, None]
    exp_sums = gather_from_all(jnp.sum(jnp.exp(logits), axis=1)[None], "row")
    totals = jnp.sum(exp_sums, axis=0)
    return logits - jnp.log(totals)[:, None]


def solution(mesh):
    placed = (
        P("row", None, "col"),
        P("row", "col"),
        P("row", "col"),
        P("row", None, "col"),
        P("row", None, "col"),
        P("row"),
        P("row"),
        P("row", None, "col"),
        P(None, "col"),
        P(None, "col", "row"),
    )
    return jax.shard_map(
        body, mesh=mesh, in_specs=placed, out_specs=P("col", "row"), check_vma=False
    )
```

```python
import jax
import jax.numpy as jnp
from jax import lax
from jax.sharding import PartitionSpec as P

HEAD_DIM = 128
D = 16384


def from_partner(value, axis, distance):
    mask = 2**distance
    pairs = [(source, source ^ mask) for source in range(lax.axis_size(axis))]
    return lax.ppermute(value, axis, pairs)


def gather_from_all(value, axis):
    size = lax.axis_size(axis)
    copies = jnp.broadcast_to(value[None], (size,) + value.shape)
    got = lax.all_to_all(copies, axis, 0, 0, tiled=True)
    return got.reshape((size * value.shape[0],) + value.shape[1:])


def split_three(value):
    high = value.astype(jnp.bfloat16)
    rest = value - high.astype(jnp.float32)
    middle = rest.astype(jnp.bfloat16)
    low = (rest - middle.astype(jnp.float32)).astype(jnp.bfloat16)
    return jnp.stack([high, middle, low], axis=-1)


def count_before(sources):
    entries = sources.shape[-1]
    earlier = jnp.arange(entries)[:, None] > jnp.arange(entries)[None, :]
    matching = sources[..., :, None] == sources[..., None, :]
    return jnp.sum(matching & earlier, axis=-1)


def attend(queries_in, key_cache, value_cache, key_new, value_new, live_rows):
    leading = queries_in.shape[:-2]
    group_size = queries_in.shape[-2]
    panel_width = queries_in.shape[-1]
    head_part = min(panel_width, HEAD_DIM)
    heads_here = panel_width // head_part
    context = key_cache.shape[-2]
    query_heads = queries_in.reshape(leading + (group_size, heads_here, head_part))
    key_heads = key_cache.reshape(leading + (context, heads_here, head_part))
    value_heads = value_cache.reshape(leading + (context, heads_here, head_part))
    fresh_key = key_new.reshape(leading + (heads_here, head_part))
    fresh_value = value_new.reshape(leading + (1, heads_here, head_part)).astype(jnp.float32)
    cached = jnp.einsum(
        "...jhe,...the->...jht", query_heads, key_heads, preferred_element_type=jnp.float32
    )
    own_score = jnp.einsum(
        "...jhe,...he->...jh", query_heads, fresh_key, preferred_element_type=jnp.float32
    )
    other_cached, other_own = from_partner((cached, own_score), "col", 0)
    cached = cached + other_cached
    own_score = own_score + other_own
    scale_factor = HEAD_DIM ** (-0.5)
    cached = cached * scale_factor
    own_score = own_score * scale_factor
    positions = lax.broadcasted_iota(jnp.int32, cached.shape, cached.ndim - 1)
    visible = positions < live_rows.reshape(leading + (1, 1, 1))
    peak_score = jnp.maximum(jnp.max(jnp.where(visible, cached, -jnp.inf), axis=-1), own_score)
    weight = jnp.where(visible, jnp.exp(cached - peak_score[..., None]), jnp.float32(0.0))
    weight_own = jnp.exp(own_score - peak_score)
    weight_sum = jnp.sum(weight, axis=-1) + weight_own
    rounded = weight.astype(jnp.bfloat16)
    rounded_own = lax.optimization_barrier(weight_own.astype(jnp.bfloat16)).astype(jnp.float32)
    summed = jnp.einsum(
        "...jht,...the->...jhe", rounded, value_heads, preferred_element_type=jnp.float32
    )
    own_part = rounded_own[..., None] * fresh_value
    result = (summed + own_part) / weight_sum[..., None]
    return result.reshape(leading + (group_size, panel_width)).astype(jnp.bfloat16)


def body(
    queries,
    new_keys,
    new_values,
    cache_keys,
    cache_values,
    lengths,
    parents,
    residual,
    norm_gain,
    vocab_weight,
):
    row_count = lax.axis_size("row")
    beam_count = parents.shape[0]
    slot_cap = max(2, (2 * beam_count + row_count - 1) // row_count)
    my_row = lax.axis_index("row")
    group_size = queries.shape[1]
    panel_width = queries.shape[2]
    source = parents // beam_count
    rank_in = count_before(source)
    slot_index = source * slot_cap + rank_in
    slot_range = jnp.arange(slot_cap, dtype=jnp.int32)
    id_table = gather_from_all(jnp.stack([parents, lengths])[None], "row")
    all_parents = id_table[:, 0].reshape(-1)
    all_lengths = id_table[:, 1].reshape(-1)
    parent_table = all_parents.reshape(row_count, beam_count)
    sources_all = parent_table // beam_count
    offsets_all = parent_table % beam_count
    ranks_all = count_before(sources_all)
    chosen = (sources_all[:, None, :] == my_row) & (
        ranks_all[:, None, :] == slot_range[None, :, None]
    )
    rows_sent = jnp.sum(jnp.where(chosen, offsets_all[:, None, :], 0), axis=2)
    sent = jnp.stack([cache_keys[rows_sent], cache_values[rows_sent]], axis=2)
    got = lax.all_to_all(sent, "row", split_axis=0, concat_axis=0, tiled=True)
    context = cache_keys.shape[1]
    kept_keys = got[:, :, 0].reshape(row_count * slot_cap, context, panel_width)[slot_index]
    kept_values = got[:, :, 1].reshape(row_count * slot_cap, context, panel_width)[slot_index]
    attended = attend(queries, kept_keys, kept_values, new_keys, new_values, all_lengths[parents])
    stream = residual.astype(jnp.float32) + attended.astype(jnp.float32)
    square_part = jnp.sum(stream * stream, axis=(1, 2))
    unscaled = (stream * norm_gain.astype(jnp.float32)[None]).astype(jnp.bfloat16)
    pieces = split_three(square_part)
    extra = jnp.zeros((beam_count, 1, panel_width), jnp.bfloat16).at[:, 0, :3].set(pieces)
    gathered = gather_from_all(jnp.concatenate([unscaled, extra], axis=1), "row")
    flat_rows = gathered[:, :group_size, :].reshape(gathered.shape[0], group_size * panel_width)
    square_all = jnp.sum(gathered[:, group_size, :3].astype(jnp.float32), axis=1)
    flat_weight = vocab_weight.reshape(group_size * panel_width, vocab_weight.shape[2])
    partial = jnp.dot(flat_rows, flat_weight, preferred_element_type=jnp.float32)
    reduced = lax.psum_scatter(partial, "col", scatter_dimension=0, tiled=True)
    col_count = lax.axis_size("col")
    square_parts = lax.all_to_all(
        square_all.reshape(col_count, -1), "col", split_axis=0, concat_axis=0, tiled=True
    )
    scaling = lax.rsqrt(jnp.sum(square_parts, axis=0) / D + 1e-05)
    logits = reduced * scaling[:, None]
    exp_sums = gather_from_all(jnp.sum(jnp.exp(logits), axis=1)[None], "row")
    totals = jnp.sum(exp_sums, axis=0)
    return logits - jnp.log(totals)[:, None]


def solution(mesh):
    placed = (
        P("row", None, "col"),
        P("row", "col"),
        P("row", "col"),
        P("row", None, "col"),
        P("row", None, "col"),
        P("row"),
        P("row"),
        P("row", None, "col"),
        P(None, "col"),
        P(None, "col", "row"),
    )
    return jax.shard_map(
        body, mesh=mesh, in_specs=placed, out_specs=P("col", "row"), check_vma=False
    )
```

```python
import jax
import jax.numpy as jnp
from jax import lax
from jax.sharding import PartitionSpec as P

HEAD_DIM = 128
D = 16384


def from_partner(value, axis, distance):
    mask = 2**distance
    pairs = [(source, source ^ mask) for source in range(lax.axis_size(axis))]
    return lax.ppermute(value, axis, pairs)


def gather_from_all(value, axis):
    size = lax.axis_size(axis)
    copies = jnp.broadcast_to(value[None], (size,) + value.shape)
    got = lax.all_to_all(copies, axis, 0, 0, tiled=True)
    return got.reshape((size * value.shape[0],) + value.shape[1:])


def split_three(value):
    high = value.astype(jnp.bfloat16)
    rest = value - high.astype(jnp.float32)
    middle = rest.astype(jnp.bfloat16)
    low = (rest - middle.astype(jnp.float32)).astype(jnp.bfloat16)
    return jnp.stack([high, middle, low], axis=-1)


def count_before(sources):
    entries = sources.shape[-1]
    earlier = jnp.arange(entries)[:, None] > jnp.arange(entries)[None, :]
    matching = sources[..., :, None] == sources[..., None, :]
    return jnp.sum(matching & earlier, axis=-1)


def attend(queries_in, key_cache, value_cache, key_new, value_new, live_rows):
    leading = queries_in.shape[:-2]
    group_size = queries_in.shape[-2]
    panel_width = queries_in.shape[-1]
    head_part = min(panel_width, HEAD_DIM)
    heads_here = panel_width // head_part
    context = key_cache.shape[-2]
    query_heads = queries_in.reshape(leading + (group_size, heads_here, head_part))
    key_heads = key_cache.reshape(leading + (context, heads_here, head_part))
    value_heads = value_cache.reshape(leading + (context, heads_here, head_part))
    fresh_key = key_new.reshape(leading + (heads_here, head_part))
    fresh_value = value_new.reshape(leading + (1, heads_here, head_part)).astype(jnp.float32)
    cached = jnp.einsum(
        "...jhe,...the->...jht", query_heads, key_heads, preferred_element_type=jnp.float32
    )
    own_score = jnp.einsum(
        "...jhe,...he->...jh", query_heads, fresh_key, preferred_element_type=jnp.float32
    )
    other_cached, other_own = from_partner((cached, own_score), "col", 0)
    cached = cached + other_cached
    own_score = own_score + other_own
    scale_factor = HEAD_DIM ** (-0.5)
    cached = cached * scale_factor
    own_score = own_score * scale_factor
    positions = lax.broadcasted_iota(jnp.int32, cached.shape, cached.ndim - 1)
    visible = positions < live_rows.reshape(leading + (1, 1, 1))
    peak_score = jnp.maximum(jnp.max(jnp.where(visible, cached, -jnp.inf), axis=-1), own_score)
    weight = jnp.where(visible, jnp.exp(cached - peak_score[..., None]), jnp.float32(0.0))
    weight_own = jnp.exp(own_score - peak_score)
    weight_sum = jnp.sum(weight, axis=-1) + weight_own
    rounded = weight.astype(jnp.bfloat16)
    rounded_own = lax.optimization_barrier(weight_own.astype(jnp.bfloat16)).astype(jnp.float32)
    summed = jnp.einsum(
        "...jht,...the->...jhe", rounded, value_heads, preferred_element_type=jnp.float32
    )
    own_part = rounded_own[..., None] * fresh_value
    result = (summed + own_part) / weight_sum[..., None]
    return result.reshape(leading + (group_size, panel_width)).astype(jnp.bfloat16)


def body(
    queries,
    new_keys,
    new_values,
    cache_keys,
    cache_values,
    lengths,
    parents,
    residual,
    norm_gain,
    vocab_weight,
):
    row_count = lax.axis_size("row")
    beam_count = parents.shape[0]
    slot_cap = max(2, (2 * beam_count + row_count - 1) // row_count)
    my_row = lax.axis_index("row")
    group_size = queries.shape[1]
    panel_width = queries.shape[2]
    source = parents // beam_count
    rank_in = count_before(source)
    slot_index = source * slot_cap + rank_in
    slot_range = jnp.arange(slot_cap, dtype=jnp.int32)
    id_table = gather_from_all(jnp.stack([parents, lengths])[None], "row")
    all_parents = id_table[:, 0].reshape(-1)
    all_lengths = id_table[:, 1].reshape(-1)
    parent_table = all_parents.reshape(row_count, beam_count)
    sources_all = parent_table // beam_count
    offsets_all = parent_table % beam_count
    ranks_all = count_before(sources_all)
    chosen = (sources_all[:, None, :] == my_row) & (
        ranks_all[:, None, :] == slot_range[None, :, None]
    )
    rows_sent = jnp.sum(jnp.where(chosen, offsets_all[:, None, :], 0), axis=2)
    sent = jnp.stack([cache_keys[rows_sent], cache_values[rows_sent]], axis=2)
    got = lax.all_to_all(sent, "row", split_axis=0, concat_axis=0, tiled=True)
    context = cache_keys.shape[1]
    kept_keys = got[:, :, 0].reshape(row_count * slot_cap, context, panel_width)[slot_index]
    kept_values = got[:, :, 1].reshape(row_count * slot_cap, context, panel_width)[slot_index]
    attended = attend(queries, kept_keys, kept_values, new_keys, new_values, all_lengths[parents])
    stream = residual.astype(jnp.float32) + attended.astype(jnp.float32)
    square_part = jnp.sum(stream * stream, axis=(1, 2))
    width = group_size * panel_width
    unscaled = (stream * norm_gain.astype(jnp.float32)[None]).astype(jnp.bfloat16)
    extra = jnp.zeros((beam_count, 128), jnp.bfloat16).at[:, :3].set(split_three(square_part))
    packed = jnp.concatenate([unscaled.reshape(beam_count, width), extra], axis=1)
    flat_weight = vocab_weight.reshape(width, vocab_weight.shape[2])
    col_count = lax.axis_size("col")
    chunks = 2
    step = beam_count // chunks
    reduced_parts, square_chunks = [], []
    for chunk in range(chunks):
        gathered = gather_from_all(packed[chunk * step : (chunk + 1) * step], "row")
        partial = jnp.dot(gathered[:, :width], flat_weight, preferred_element_type=jnp.float32)
        reduced = lax.psum_scatter(partial, "col", scatter_dimension=0, tiled=True)
        reduced_parts.append(reduced.reshape(-1, step, reduced.shape[-1]))
        squares = jnp.sum(gathered[:, width : width + 3].astype(jnp.float32), axis=1)
        square_chunks.append(squares.reshape(col_count, -1, step))
    reduced = jnp.stack(reduced_parts, axis=1).reshape(-1, flat_weight.shape[1])
    square_all = jnp.stack(square_chunks, axis=2).reshape(col_count, -1)
    square_parts = lax.all_to_all(square_all, "col", split_axis=0, concat_axis=0, tiled=True)
    scaling = lax.rsqrt(jnp.sum(square_parts, axis=0) / D + 1e-05)
    logits = reduced * scaling[:, None]
    exp_sums = gather_from_all(jnp.sum(jnp.exp(logits), axis=1)[None], "row")
    totals = jnp.sum(exp_sums, axis=0)
    return logits - jnp.log(totals)[:, None]


def solution(mesh):
    placed = (
        P("row", None, "col"),
        P("row", "col"),
        P("row", "col"),
        P("row", None, "col"),
        P("row", None, "col"),
        P("row"),
        P("row"),
        P("row", None, "col"),
        P(None, "col"),
        P(None, "col", "row"),
    )
    return jax.shard_map(
        body, mesh=mesh, in_specs=placed, out_specs=P("col", "row"), check_vma=False
    )
```

```python
import jax
import jax.numpy as jnp
from jax import lax
from jax.sharding import PartitionSpec as P

HEAD_DIM = 128
D = 16384


def from_partner(value, axis, distance):
    mask = 2**distance
    pairs = [(source, source ^ mask) for source in range(lax.axis_size(axis))]
    return lax.ppermute(value, axis, pairs)


def gather_from_all(value, axis):
    size = lax.axis_size(axis)
    copies = jnp.broadcast_to(value[None], (size,) + value.shape)
    got = lax.all_to_all(copies, axis, 0, 0, tiled=True)
    return got.reshape((size * value.shape[0],) + value.shape[1:])


def split_three(value):
    high = value.astype(jnp.bfloat16)
    rest = value - high.astype(jnp.float32)
    middle = rest.astype(jnp.bfloat16)
    low = (rest - middle.astype(jnp.float32)).astype(jnp.bfloat16)
    return jnp.stack([high, middle, low], axis=-1)


def count_before(sources):
    entries = sources.shape[-1]
    earlier = jnp.arange(entries)[:, None] > jnp.arange(entries)[None, :]
    matching = sources[..., :, None] == sources[..., None, :]
    return jnp.sum(matching & earlier, axis=-1)


def attend(queries_in, key_cache, value_cache, key_new, value_new, live_rows):
    leading = queries_in.shape[:-2]
    group_size = queries_in.shape[-2]
    panel_width = queries_in.shape[-1]
    head_part = min(panel_width, HEAD_DIM)
    heads_here = panel_width // head_part
    context = key_cache.shape[-2]
    query_heads = queries_in.reshape(leading + (group_size, heads_here, head_part))
    key_heads = key_cache.reshape(leading + (context, heads_here, head_part))
    value_heads = value_cache.reshape(leading + (context, heads_here, head_part))
    fresh_key = key_new.reshape(leading + (heads_here, head_part))
    fresh_value = value_new.reshape(leading + (1, heads_here, head_part)).astype(jnp.float32)
    cached = jnp.einsum(
        "...jhe,...the->...jht", query_heads, key_heads, preferred_element_type=jnp.float32
    )
    own_score = jnp.einsum(
        "...jhe,...he->...jh", query_heads, fresh_key, preferred_element_type=jnp.float32
    )
    other_cached, other_own = from_partner((cached, own_score), "col", 0)
    cached = cached + other_cached
    own_score = own_score + other_own
    scale_factor = HEAD_DIM ** (-0.5)
    cached = cached * scale_factor
    own_score = own_score * scale_factor
    positions = lax.broadcasted_iota(jnp.int32, cached.shape, cached.ndim - 1)
    visible = positions < live_rows.reshape(leading + (1, 1, 1))
    peak_score = jnp.maximum(jnp.max(jnp.where(visible, cached, -jnp.inf), axis=-1), own_score)
    weight = jnp.where(visible, jnp.exp(cached - peak_score[..., None]), jnp.float32(0.0))
    weight_own = jnp.exp(own_score - peak_score)
    weight_sum = jnp.sum(weight, axis=-1) + weight_own
    rounded = weight.astype(jnp.bfloat16)
    rounded_own = lax.optimization_barrier(weight_own.astype(jnp.bfloat16)).astype(jnp.float32)
    summed = jnp.einsum(
        "...jht,...the->...jhe", rounded, value_heads, preferred_element_type=jnp.float32
    )
    own_part = rounded_own[..., None] * fresh_value
    result = (summed + own_part) / weight_sum[..., None]
    return result.reshape(leading + (group_size, panel_width)).astype(jnp.bfloat16)


def body(
    queries,
    new_keys,
    new_values,
    cache_keys,
    cache_values,
    lengths,
    parents,
    residual,
    norm_gain,
    vocab_weight,
):
    row_count = lax.axis_size("row")
    beam_count = parents.shape[0]
    slot_cap = max(2, (2 * beam_count + row_count - 1) // row_count)
    group_size = queries.shape[1]
    panel_width = queries.shape[2]
    source = parents // beam_count
    rank_in = count_before(source)
    offset_row = jnp.broadcast_to(
        (parents % beam_count).astype(jnp.bfloat16)[:, None, None], (beam_count, 1, panel_width)
    )
    message = jnp.concatenate(
        [queries, new_keys[:, None, :], new_values[:, None, :], offset_row], axis=1
    )
    outgoing = jnp.zeros((row_count, slot_cap) + message.shape[1:], message.dtype)
    outgoing = outgoing.at[source, rank_in].set(message)
    incoming = lax.all_to_all(outgoing, "row", split_axis=0, concat_axis=0, tiled=True)
    incoming = incoming.reshape((row_count * slot_cap,) + message.shape[1:])
    offsets = incoming[:, group_size + 2, 0].astype(jnp.int32)
    served = attend(
        incoming[:, :group_size],
        cache_keys[offsets],
        cache_values[offsets],
        incoming[:, group_size],
        incoming[:, group_size + 1],
        lengths[offsets],
    )
    returned = lax.all_to_all(
        served.reshape((row_count, slot_cap) + served.shape[1:]),
        "row",
        split_axis=0,
        concat_axis=0,
        tiled=True,
    )
    attended = returned[source, rank_in]
    stream = residual.astype(jnp.float32) + attended.astype(jnp.float32)
    square_part = jnp.sum(stream * stream, axis=(1, 2))
    unscaled = (stream * norm_gain.astype(jnp.float32)[None]).astype(jnp.bfloat16)
    pieces = split_three(square_part)
    extra = jnp.zeros((beam_count, 1, panel_width), jnp.bfloat16).at[:, 0, :3].set(pieces)
    gathered = gather_from_all(jnp.concatenate([unscaled, extra], axis=1), "row")
    flat_rows = gathered[:, :group_size, :].reshape(gathered.shape[0], group_size * panel_width)
    square_all = jnp.sum(gathered[:, group_size, :3].astype(jnp.float32), axis=1)
    flat_weight = vocab_weight.reshape(group_size * panel_width, vocab_weight.shape[2])
    partial = jnp.dot(flat_rows, flat_weight, preferred_element_type=jnp.float32)
    reduced = lax.psum_scatter(partial, "col", scatter_dimension=0, tiled=True)
    col_count = lax.axis_size("col")
    square_parts = lax.all_to_all(
        square_all.reshape(col_count, -1), "col", split_axis=0, concat_axis=0, tiled=True
    )
    scaling = lax.rsqrt(jnp.sum(square_parts, axis=0) / D + 1e-05)
    logits = reduced * scaling[:, None]
    exp_sums = gather_from_all(jnp.sum(jnp.exp(logits), axis=1)[None], "row")
    totals = jnp.sum(exp_sums, axis=0)
    return logits - jnp.log(totals)[:, None]


def solution(mesh):
    placed = (
        P("row", None, "col"),
        P("row", "col"),
        P("row", "col"),
        P("row", None, "col"),
        P("row", None, "col"),
        P("row"),
        P("row"),
        P("row", None, "col"),
        P(None, "col"),
        P(None, "col", "row"),
    )
    return jax.shard_map(
        body, mesh=mesh, in_specs=placed, out_specs=P("col", "row"), check_vma=False
    )
```

```python
import jax
import jax.numpy as jnp
from jax import lax
from jax.sharding import PartitionSpec as P

HEAD_DIM = 128
D = 16384


def from_partner(value, axis, distance):
    mask = 2**distance
    pairs = [(source, source ^ mask) for source in range(lax.axis_size(axis))]
    return lax.ppermute(value, axis, pairs)


def gather_from_all(value, axis):
    size = lax.axis_size(axis)
    copies = jnp.broadcast_to(value[None], (size,) + value.shape)
    got = lax.all_to_all(copies, axis, 0, 0, tiled=True)
    return got.reshape((size * value.shape[0],) + value.shape[1:])


def split_three(value):
    high = value.astype(jnp.bfloat16)
    rest = value - high.astype(jnp.float32)
    middle = rest.astype(jnp.bfloat16)
    low = (rest - middle.astype(jnp.float32)).astype(jnp.bfloat16)
    return jnp.stack([high, middle, low], axis=-1)


def count_before(sources):
    entries = sources.shape[-1]
    earlier = jnp.arange(entries)[:, None] > jnp.arange(entries)[None, :]
    matching = sources[..., :, None] == sources[..., None, :]
    return jnp.sum(matching & earlier, axis=-1)


def attend(queries_in, key_cache, value_cache, key_new, value_new, live_rows):
    leading = queries_in.shape[:-2]
    group_size = queries_in.shape[-2]
    panel_width = queries_in.shape[-1]
    head_part = min(panel_width, HEAD_DIM)
    heads_here = panel_width // head_part
    context = key_cache.shape[-2]
    query_heads = queries_in.reshape(leading + (group_size, heads_here, head_part))
    key_heads = key_cache.reshape(leading + (context, heads_here, head_part))
    value_heads = value_cache.reshape(leading + (context, heads_here, head_part))
    fresh_key = key_new.reshape(leading + (heads_here, head_part))
    fresh_value = value_new.reshape(leading + (1, heads_here, head_part)).astype(jnp.float32)
    cached = jnp.einsum(
        "...jhe,...the->...jht", query_heads, key_heads, preferred_element_type=jnp.float32
    )
    own_score = jnp.einsum(
        "...jhe,...he->...jh", query_heads, fresh_key, preferred_element_type=jnp.float32
    )
    other_cached, other_own = from_partner((cached, own_score), "col", 0)
    cached = cached + other_cached
    own_score = own_score + other_own
    scale_factor = HEAD_DIM ** (-0.5)
    cached = cached * scale_factor
    own_score = own_score * scale_factor
    positions = lax.broadcasted_iota(jnp.int32, cached.shape, cached.ndim - 1)
    visible = positions < live_rows.reshape(leading + (1, 1, 1))
    peak_score = jnp.maximum(jnp.max(jnp.where(visible, cached, -jnp.inf), axis=-1), own_score)
    weight = jnp.where(visible, jnp.exp(cached - peak_score[..., None]), jnp.float32(0.0))
    weight_own = jnp.exp(own_score - peak_score)
    weight_sum = jnp.sum(weight, axis=-1) + weight_own
    rounded = weight.astype(jnp.bfloat16)
    rounded_own = lax.optimization_barrier(weight_own.astype(jnp.bfloat16)).astype(jnp.float32)
    summed = jnp.einsum(
        "...jht,...the->...jhe", rounded, value_heads, preferred_element_type=jnp.float32
    )
    own_part = rounded_own[..., None] * fresh_value
    result = (summed + own_part) / weight_sum[..., None]
    return result.reshape(leading + (group_size, panel_width)).astype(jnp.bfloat16)


def body(
    queries,
    new_keys,
    new_values,
    cache_keys,
    cache_values,
    lengths,
    parents,
    residual,
    norm_gain,
    vocab_weight,
):
    row_count = lax.axis_size("row")
    beam_count = parents.shape[0]
    slot_cap = max(2, (2 * beam_count + row_count - 1) // row_count)
    group_size = queries.shape[1]
    panel_width = queries.shape[2]
    source = parents // beam_count
    rank_in = count_before(source)
    offset_row = jnp.broadcast_to(
        (parents % beam_count).astype(jnp.bfloat16)[:, None, None], (beam_count, 1, panel_width)
    )
    message = jnp.concatenate(
        [queries, new_keys[:, None, :], new_values[:, None, :], offset_row], axis=1
    )
    outgoing = jnp.zeros((row_count, slot_cap) + message.shape[1:], message.dtype)
    outgoing = outgoing.at[source, rank_in].set(message)
    incoming = lax.all_to_all(outgoing, "row", split_axis=0, concat_axis=0, tiled=True)
    incoming = incoming.reshape((row_count * slot_cap,) + message.shape[1:])
    offsets = incoming[:, group_size + 2, 0].astype(jnp.int32)
    served = attend(
        incoming[:, :group_size],
        cache_keys[offsets],
        cache_values[offsets],
        incoming[:, group_size],
        incoming[:, group_size + 1],
        lengths[offsets],
    )
    returned = lax.all_to_all(
        served.reshape((row_count, slot_cap) + served.shape[1:]),
        "row",
        split_axis=0,
        concat_axis=0,
        tiled=True,
    )
    attended = returned[source, rank_in]
    stream = residual.astype(jnp.float32) + attended.astype(jnp.float32)
    square_part = jnp.sum(stream * stream, axis=(1, 2))
    width = group_size * panel_width
    unscaled = (stream * norm_gain.astype(jnp.float32)[None]).astype(jnp.bfloat16)
    extra = jnp.zeros((beam_count, 128), jnp.bfloat16).at[:, :3].set(split_three(square_part))
    packed = jnp.concatenate([unscaled.reshape(beam_count, width), extra], axis=1)
    gathered = gather_from_all(packed, "row")
    flat_rows = gathered[:, :width]
    square_all = jnp.sum(gathered[:, width : width + 3].astype(jnp.float32), axis=1)
    flat_weight = vocab_weight.reshape(width, vocab_weight.shape[2])
    partial = jnp.dot(flat_rows, flat_weight, preferred_element_type=jnp.float32)
    reduced = lax.psum_scatter(partial, "col", scatter_dimension=0, tiled=True)
    col_count = lax.axis_size("col")
    square_parts = lax.all_to_all(
        square_all.reshape(col_count, -1), "col", split_axis=0, concat_axis=0, tiled=True
    )
    scaling = lax.rsqrt(jnp.sum(square_parts, axis=0) / D + 1e-05)
    logits = reduced * scaling[:, None]
    exp_sums = gather_from_all(jnp.sum(jnp.exp(logits), axis=1)[None], "row")
    totals = jnp.sum(exp_sums, axis=0)
    return logits - jnp.log(totals)[:, None]


def solution(mesh):
    placed = (
        P("row", None, "col"),
        P("row", "col"),
        P("row", "col"),
        P("row", None, "col"),
        P("row", None, "col"),
        P("row"),
        P("row"),
        P("row", None, "col"),
        P(None, "col"),
        P(None, "col", "row"),
    )
    return jax.shard_map(
        body, mesh=mesh, in_specs=placed, out_specs=P("col", "row"), check_vma=False
    )
```

```python
import jax
import jax.numpy as jnp
from jax import lax
from jax.sharding import PartitionSpec as P

HEAD_DIM = 128
D = 16384


def from_partner(value, axis, distance):
    mask = 2**distance
    pairs = [(source, source ^ mask) for source in range(lax.axis_size(axis))]
    return lax.ppermute(value, axis, pairs)


def gather_from_all(value, axis):
    size = lax.axis_size(axis)
    copies = jnp.broadcast_to(value[None], (size,) + value.shape)
    got = lax.all_to_all(copies, axis, 0, 0, tiled=True)
    return got.reshape((size * value.shape[0],) + value.shape[1:])


def split_three(value):
    high = value.astype(jnp.bfloat16)
    rest = value - high.astype(jnp.float32)
    middle = rest.astype(jnp.bfloat16)
    low = (rest - middle.astype(jnp.float32)).astype(jnp.bfloat16)
    return jnp.stack([high, middle, low], axis=-1)


def count_before(sources):
    entries = sources.shape[-1]
    earlier = jnp.arange(entries)[:, None] > jnp.arange(entries)[None, :]
    matching = sources[..., :, None] == sources[..., None, :]
    return jnp.sum(matching & earlier, axis=-1)


def attend(query_full, key_full, value_half, key_new, value_new, live_rows):
    scale_factor = HEAD_DIM ** (-0.5)
    cached = jnp.einsum(
        "sjd,std->sjt", query_full, key_full, preferred_element_type=jnp.float32
    ) * scale_factor
    own_score = jnp.einsum(
        "sjd,sd->sj", query_full, key_new, preferred_element_type=jnp.float32
    ) * scale_factor
    positions = lax.broadcasted_iota(jnp.int32, cached.shape, cached.ndim - 1)
    visible = positions < live_rows[:, None, None]
    peak_score = jnp.maximum(jnp.max(jnp.where(visible, cached, -jnp.inf), axis=-1), own_score)
    weight = jnp.where(visible, jnp.exp(cached - peak_score[..., None]), jnp.float32(0.0))
    weight_own = jnp.exp(own_score - peak_score)
    weight_sum = jnp.sum(weight, axis=-1) + weight_own
    rounded = weight.astype(jnp.bfloat16)
    rounded_own = lax.optimization_barrier(weight_own.astype(jnp.bfloat16)).astype(jnp.float32)
    summed = jnp.einsum("sjt,ste->sje", rounded, value_half, preferred_element_type=jnp.float32)
    own_part = rounded_own[..., None] * value_new.astype(jnp.float32)[:, None, :]
    return ((summed + own_part) / weight_sum[..., None]).astype(jnp.bfloat16)


def body(
    queries,
    new_keys,
    new_values,
    cache_keys,
    cache_values,
    lengths,
    parents,
    residual,
    norm_gain,
    vocab_weight,
):
    row_count = lax.axis_size("row")
    beam_count = parents.shape[0]
    slot_cap = max(2, (2 * beam_count + row_count - 1) // row_count)
    group_size = queries.shape[1]
    panel_width = queries.shape[2]
    source = parents // beam_count
    rank_in = count_before(source)
    other_queries, other_new_keys, other_keys = from_partner(
        (queries, new_keys, cache_keys), "col", 0
    )
    offset_part = jnp.broadcast_to(
        (parents % beam_count).astype(jnp.bfloat16)[:, None], (beam_count, panel_width)
    )
    message = jnp.concatenate(
        [
            jnp.concatenate([queries, other_queries], axis=-1),
            jnp.concatenate([new_keys, other_new_keys], axis=-1)[:, None, :],
            jnp.concatenate([new_values, offset_part], axis=-1)[:, None, :],
        ],
        axis=1,
    )
    outgoing = jnp.zeros((row_count, slot_cap) + message.shape[1:], message.dtype)
    outgoing = outgoing.at[source, rank_in].set(message)
    incoming = lax.all_to_all(outgoing, "row", split_axis=0, concat_axis=0, tiled=True)
    incoming = incoming.reshape((row_count * slot_cap,) + message.shape[1:])
    offsets = incoming[:, group_size + 1, panel_width].astype(jnp.int32)
    whole_keys = jnp.concatenate([cache_keys, other_keys], axis=-1)
    served = attend(
        incoming[:, :group_size],
        whole_keys[offsets],
        cache_values[offsets],
        incoming[:, group_size],
        incoming[:, group_size + 1, :panel_width],
        lengths[offsets],
    )
    returned = lax.all_to_all(
        served.reshape((row_count, slot_cap) + served.shape[1:]),
        "row",
        split_axis=0,
        concat_axis=0,
        tiled=True,
    )
    attended = returned[source, rank_in]
    stream = residual.astype(jnp.float32) + attended.astype(jnp.float32)
    square_part = jnp.sum(stream * stream, axis=(1, 2))
    width = group_size * panel_width
    unscaled = (stream * norm_gain.astype(jnp.float32)[None]).astype(jnp.bfloat16)
    extra = jnp.zeros((beam_count, 128), jnp.bfloat16).at[:, :3].set(split_three(square_part))
    packed = jnp.concatenate([unscaled.reshape(beam_count, width), extra], axis=1)
    gathered = gather_from_all(packed, "row")
    flat_rows = gathered[:, :width]
    square_all = jnp.sum(gathered[:, width : width + 3].astype(jnp.float32), axis=1)
    flat_weight = vocab_weight.reshape(width, vocab_weight.shape[2])
    partial = jnp.dot(flat_rows, flat_weight, preferred_element_type=jnp.float32)
    reduced = lax.psum_scatter(partial, "col", scatter_dimension=0, tiled=True)
    col_count = lax.axis_size("col")
    square_parts = lax.all_to_all(
        square_all.reshape(col_count, -1), "col", split_axis=0, concat_axis=0, tiled=True
    )
    scaling = lax.rsqrt(jnp.sum(square_parts, axis=0) / D + 1e-05)
    logits = reduced * scaling[:, None]
    exp_sums = gather_from_all(jnp.sum(jnp.exp(logits), axis=1)[None], "row")
    totals = jnp.sum(exp_sums, axis=0)
    return logits - jnp.log(totals)[:, None]


def solution(mesh):
    placed = (
        P("row", None, "col"),
        P("row", "col"),
        P("row", "col"),
        P("row", None, "col"),
        P("row", None, "col"),
        P("row"),
        P("row"),
        P("row", None, "col"),
        P(None, "col"),
        P(None, "col", "row"),
    )
    return jax.shard_map(
        body, mesh=mesh, in_specs=placed, out_specs=P("col", "row"), check_vma=False
    )
```

```python
import jax
import jax.numpy as jnp
from jax import lax
from jax.sharding import PartitionSpec as P

HEAD_DIM = 128
COL = ("high", "low")
D = 16384


def from_partner(value, axis, distance):
    mask = 2**distance
    pairs = [(source, source ^ mask) for source in range(lax.axis_size(axis))]
    return lax.ppermute(value, axis, pairs)


def gather_from_all(value, axis):
    size = lax.axis_size(axis)
    copies = jnp.broadcast_to(value[None], (size,) + value.shape)
    got = lax.all_to_all(copies, axis, 0, 0, tiled=True)
    return got.reshape((size * value.shape[0],) + value.shape[1:])


def split_three(value):
    high = value.astype(jnp.bfloat16)
    rest = value - high.astype(jnp.float32)
    middle = rest.astype(jnp.bfloat16)
    low = (rest - middle.astype(jnp.float32)).astype(jnp.bfloat16)
    return jnp.stack([high, middle, low], axis=-1)


def count_before(sources):
    entries = sources.shape[-1]
    earlier = jnp.arange(entries)[:, None] > jnp.arange(entries)[None, :]
    matching = sources[..., :, None] == sources[..., None, :]
    return jnp.sum(matching & earlier, axis=-1)


def attend(query_full, key_full, value_half, key_new, value_new, live_rows):
    scale_factor = HEAD_DIM ** (-0.5)
    cached = jnp.einsum(
        "sjd,std->sjt", query_full, key_full, preferred_element_type=jnp.float32
    ) * scale_factor
    own_score = jnp.einsum(
        "sjd,sd->sj", query_full, key_new, preferred_element_type=jnp.float32
    ) * scale_factor
    positions = lax.broadcasted_iota(jnp.int32, cached.shape, cached.ndim - 1)
    visible = positions < live_rows[:, None, None]
    peak_score = jnp.maximum(jnp.max(jnp.where(visible, cached, -jnp.inf), axis=-1), own_score)
    weight = jnp.where(visible, jnp.exp(cached - peak_score[..., None]), jnp.float32(0.0))
    weight_own = jnp.exp(own_score - peak_score)
    weight_sum = jnp.sum(weight, axis=-1) + weight_own
    rounded = weight.astype(jnp.bfloat16)
    rounded_own = lax.optimization_barrier(weight_own.astype(jnp.bfloat16)).astype(jnp.float32)
    summed = jnp.einsum("sjt,ste->sje", rounded, value_half, preferred_element_type=jnp.float32)
    own_part = rounded_own[..., None] * value_new.astype(jnp.float32)[:, None, :]
    return ((summed + own_part) / weight_sum[..., None]).astype(jnp.bfloat16)


def body(
    queries,
    new_keys,
    new_values,
    cache_keys,
    cache_values,
    lengths,
    parents,
    residual,
    norm_gain,
    vocab_weight,
):
    row_count = lax.axis_size("row")
    beam_count = parents.shape[0]
    slot_cap = max(2, (2 * beam_count + row_count - 1) // row_count)
    group_size = queries.shape[1]
    panel_width = queries.shape[2]
    source = parents // beam_count
    rank_in = count_before(source)
    other_queries, other_new_keys, other_keys = from_partner(
        (queries, new_keys, cache_keys), "low", 0
    )
    offset_part = jnp.broadcast_to(
        (parents % beam_count).astype(jnp.bfloat16)[:, None], (beam_count, panel_width)
    )
    message = jnp.concatenate(
        [
            jnp.concatenate([queries, other_queries], axis=-1),
            jnp.concatenate([new_keys, other_new_keys], axis=-1)[:, None, :],
            jnp.concatenate([new_values, offset_part], axis=-1)[:, None, :],
        ],
        axis=1,
    )
    outgoing = jnp.zeros((row_count, slot_cap) + message.shape[1:], message.dtype)
    outgoing = outgoing.at[source, rank_in].set(message)
    incoming = lax.all_to_all(outgoing, "row", split_axis=0, concat_axis=0, tiled=True)
    incoming = incoming.reshape((row_count * slot_cap,) + message.shape[1:])
    offsets = incoming[:, group_size + 1, panel_width].astype(jnp.int32)
    whole_keys = jnp.concatenate([cache_keys, other_keys], axis=-1)
    served = attend(
        incoming[:, :group_size],
        whole_keys[offsets],
        cache_values[offsets],
        incoming[:, group_size],
        incoming[:, group_size + 1, :panel_width],
        lengths[offsets],
    )
    returned = lax.all_to_all(
        served.reshape((row_count, slot_cap) + served.shape[1:]),
        "row",
        split_axis=0,
        concat_axis=0,
        tiled=True,
    )
    attended = returned[source, rank_in]
    stream = residual.astype(jnp.float32) + attended.astype(jnp.float32)
    square_part = jnp.sum(stream * stream, axis=(1, 2))
    width = group_size * panel_width
    unscaled = (stream * norm_gain.astype(jnp.float32)[None]).astype(jnp.bfloat16)
    extra = jnp.zeros((beam_count, 128), jnp.bfloat16).at[:, :3].set(split_three(square_part))
    packed = jnp.concatenate([unscaled.reshape(beam_count, width), extra], axis=1)
    gathered = gather_from_all(packed, "row")
    flat_rows = gathered[:, :width]
    square_all = jnp.sum(gathered[:, width : width + 3].astype(jnp.float32), axis=1)
    flat_weight = vocab_weight.reshape(width, vocab_weight.shape[2])
    partial = jnp.dot(flat_rows, flat_weight, preferred_element_type=jnp.float32)
    high_count, low_count = lax.axis_size("high"), lax.axis_size("low")
    col_count = high_count * low_count
    blocks = partial.reshape(high_count, low_count, -1, partial.shape[1])
    by_low = jnp.swapaxes(blocks, 0, 1).reshape(partial.shape)
    reduced = lax.psum_scatter(by_low, "low", scatter_dimension=0, tiled=True)
    reduced = lax.psum_scatter(reduced, "high", scatter_dimension=0, tiled=True)
    square_parts = lax.all_to_all(
        square_all.reshape(col_count, -1), COL, split_axis=0, concat_axis=0, tiled=True
    )
    scaling = lax.rsqrt(jnp.sum(square_parts, axis=0) / D + 1e-05)
    logits = reduced * scaling[:, None]
    exp_sums = gather_from_all(jnp.sum(jnp.exp(logits), axis=1)[None], "row")
    totals = jnp.sum(exp_sums, axis=0)
    return logits - jnp.log(totals)[:, None]


def solution(mesh):
    rows, cols = mesh.devices.shape
    split = jax.sharding.Mesh(mesh.devices.reshape(rows, 4, cols // 4), ("row",) + COL)
    placed = (
        P("row", None, COL),
        P("row", COL),
        P("row", COL),
        P("row", None, COL),
        P("row", None, COL),
        P("row"),
        P("row"),
        P("row", None, COL),
        P(None, COL),
        P(None, COL, "row"),
    )
    return jax.shard_map(
        body, mesh=split, in_specs=placed, out_specs=P(COL, "row"), check_vma=False
    )
```

```python
import jax
import jax.numpy as jnp
from jax import lax
from jax.sharding import PartitionSpec as P

HEAD_DIM = 128
D = 16384


def from_partner(value, axis, distance):
    mask = 2**distance
    pairs = [(source, source ^ mask) for source in range(lax.axis_size(axis))]
    return lax.ppermute(value, axis, pairs)


def gather_from_all(value, axis):
    size = lax.axis_size(axis)
    copies = jnp.broadcast_to(value[None], (size,) + value.shape)
    got = lax.all_to_all(copies, axis, 0, 0, tiled=True)
    return got.reshape((size * value.shape[0],) + value.shape[1:])


def ring_reduce_scatter(value, axis):
    size = lax.axis_size(axis)
    me = lax.axis_index(axis)
    rows = value.shape[0] // size
    half = value.shape[1] // 2
    lanes = (value[:, :half], value[:, half:])
    shifts = (1, size - 1)
    moving = [None, None]
    for step in range(size):
        for lane in range(2):
            block = (me - shifts[lane] * (step + 1)) % size
            own = lax.dynamic_slice_in_dim(lanes[lane], block * rows, rows, axis=0)
            moving[lane] = own if step == 0 else moving[lane] + own
            if step < size - 1:
                pairs = [(source, (source + shifts[lane]) % size) for source in range(size)]
                moving[lane] = lax.ppermute(moving[lane], axis, pairs)
    return jnp.concatenate(moving, axis=1)


def split_three(value):
    high = value.astype(jnp.bfloat16)
    rest = value - high.astype(jnp.float32)
    middle = rest.astype(jnp.bfloat16)
    low = (rest - middle.astype(jnp.float32)).astype(jnp.bfloat16)
    return jnp.stack([high, middle, low], axis=-1)


def count_before(sources):
    entries = sources.shape[-1]
    earlier = jnp.arange(entries)[:, None] > jnp.arange(entries)[None, :]
    matching = sources[..., :, None] == sources[..., None, :]
    return jnp.sum(matching & earlier, axis=-1)


def attend(query_full, key_full, value_half, key_new, value_new, live_rows):
    scale_factor = HEAD_DIM ** (-0.5)
    cached = jnp.einsum(
        "sjd,std->sjt", query_full, key_full, preferred_element_type=jnp.float32
    ) * scale_factor
    own_score = jnp.einsum(
        "sjd,sd->sj", query_full, key_new, preferred_element_type=jnp.float32
    ) * scale_factor
    positions = lax.broadcasted_iota(jnp.int32, cached.shape, cached.ndim - 1)
    visible = positions < live_rows[:, None, None]
    peak_score = jnp.maximum(jnp.max(jnp.where(visible, cached, -jnp.inf), axis=-1), own_score)
    weight = jnp.where(visible, jnp.exp(cached - peak_score[..., None]), jnp.float32(0.0))
    weight_own = jnp.exp(own_score - peak_score)
    weight_sum = jnp.sum(weight, axis=-1) + weight_own
    rounded = weight.astype(jnp.bfloat16)
    rounded_own = lax.optimization_barrier(weight_own.astype(jnp.bfloat16)).astype(jnp.float32)
    summed = jnp.einsum("sjt,ste->sje", rounded, value_half, preferred_element_type=jnp.float32)
    own_part = rounded_own[..., None] * value_new.astype(jnp.float32)[:, None, :]
    return ((summed + own_part) / weight_sum[..., None]).astype(jnp.bfloat16)


def body(
    queries,
    new_keys,
    new_values,
    cache_keys,
    cache_values,
    lengths,
    parents,
    residual,
    norm_gain,
    vocab_weight,
):
    row_count = lax.axis_size("row")
    beam_count = parents.shape[0]
    slot_cap = max(2, (2 * beam_count + row_count - 1) // row_count)
    group_size = queries.shape[1]
    panel_width = queries.shape[2]
    source = parents // beam_count
    rank_in = count_before(source)
    other_queries, other_new_keys, other_keys = from_partner(
        (queries, new_keys, cache_keys), "col", 0
    )
    offset_part = jnp.broadcast_to(
        (parents % beam_count).astype(jnp.bfloat16)[:, None], (beam_count, panel_width)
    )
    message = jnp.concatenate(
        [
            jnp.concatenate([queries, other_queries], axis=-1),
            jnp.concatenate([new_keys, other_new_keys], axis=-1)[:, None, :],
            jnp.concatenate([new_values, offset_part], axis=-1)[:, None, :],
        ],
        axis=1,
    )
    outgoing = jnp.zeros((row_count, slot_cap) + message.shape[1:], message.dtype)
    outgoing = outgoing.at[source, rank_in].set(message)
    incoming = lax.all_to_all(outgoing, "row", split_axis=0, concat_axis=0, tiled=True)
    incoming = incoming.reshape((row_count * slot_cap,) + message.shape[1:])
    offsets = incoming[:, group_size + 1, panel_width].astype(jnp.int32)
    whole_keys = jnp.concatenate([cache_keys, other_keys], axis=-1)
    served = attend(
        incoming[:, :group_size],
        whole_keys[offsets],
        cache_values[offsets],
        incoming[:, group_size],
        incoming[:, group_size + 1, :panel_width],
        lengths[offsets],
    )
    returned = lax.all_to_all(
        served.reshape((row_count, slot_cap) + served.shape[1:]),
        "row",
        split_axis=0,
        concat_axis=0,
        tiled=True,
    )
    attended = returned[source, rank_in]
    stream = residual.astype(jnp.float32) + attended.astype(jnp.float32)
    square_part = jnp.sum(stream * stream, axis=(1, 2))
    width = group_size * panel_width
    unscaled = (stream * norm_gain.astype(jnp.float32)[None]).astype(jnp.bfloat16)
    extra = jnp.zeros((beam_count, 128), jnp.bfloat16).at[:, :3].set(split_three(square_part))
    packed = jnp.concatenate([unscaled.reshape(beam_count, width), extra], axis=1)
    gathered = gather_from_all(packed, "row")
    flat_rows = gathered[:, :width]
    square_all = jnp.sum(gathered[:, width : width + 3].astype(jnp.float32), axis=1)
    flat_weight = vocab_weight.reshape(width, vocab_weight.shape[2])
    partial = jnp.dot(flat_rows, flat_weight, preferred_element_type=jnp.float32)
    col_count = lax.axis_size("col")
    reduced = ring_reduce_scatter(partial, "col")
    square_parts = lax.all_to_all(
        square_all.reshape(col_count, -1), "col", split_axis=0, concat_axis=0, tiled=True
    )
    scaling = lax.rsqrt(jnp.sum(square_parts, axis=0) / D + 1e-05)
    logits = reduced * scaling[:, None]
    exp_sums = gather_from_all(jnp.sum(jnp.exp(logits), axis=1)[None], "row")
    totals = jnp.sum(exp_sums, axis=0)
    return logits - jnp.log(totals)[:, None]


def solution(mesh):
    placed = (
        P("row", None, "col"),
        P("row", "col"),
        P("row", "col"),
        P("row", None, "col"),
        P("row", None, "col"),
        P("row"),
        P("row"),
        P("row", None, "col"),
        P(None, "col"),
        P(None, "col", "row"),
    )
    return jax.shard_map(
        body, mesh=mesh, in_specs=placed, out_specs=P("col", "row"), check_vma=False
    )
```

```python
import jax
import jax.numpy as jnp
from jax import lax
from jax.sharding import PartitionSpec as P

HEAD_DIM = 128
D = 16384


def from_partner(value, axis, distance):
    mask = 2**distance
    pairs = [(source, source ^ mask) for source in range(lax.axis_size(axis))]
    return lax.ppermute(value, axis, pairs)


def gather_from_all(value, axis):
    size = lax.axis_size(axis)
    copies = jnp.broadcast_to(value[None], (size,) + value.shape)
    got = lax.all_to_all(copies, axis, 0, 0, tiled=True)
    return got.reshape((size * value.shape[0],) + value.shape[1:])


def split_three(value):
    high = value.astype(jnp.bfloat16)
    rest = value - high.astype(jnp.float32)
    middle = rest.astype(jnp.bfloat16)
    low = (rest - middle.astype(jnp.float32)).astype(jnp.bfloat16)
    return jnp.stack([high, middle, low], axis=-1)


def count_before(sources):
    entries = sources.shape[-1]
    earlier = jnp.arange(entries)[:, None] > jnp.arange(entries)[None, :]
    matching = sources[..., :, None] == sources[..., None, :]
    return jnp.sum(matching & earlier, axis=-1)


def attend(query_full, key_full, value_half, key_new, value_new, live_rows):
    scale_factor = HEAD_DIM ** (-0.5)
    cached = jnp.einsum(
        "sjd,std->sjt", query_full, key_full, preferred_element_type=jnp.float32
    ) * scale_factor
    own_score = jnp.einsum(
        "sjd,sd->sj", query_full, key_new, preferred_element_type=jnp.float32
    ) * scale_factor
    positions = lax.broadcasted_iota(jnp.int32, cached.shape, cached.ndim - 1)
    visible = positions < live_rows[:, None, None]
    peak_score = jnp.maximum(jnp.max(jnp.where(visible, cached, -jnp.inf), axis=-1), own_score)
    weight = jnp.where(visible, jnp.exp(cached - peak_score[..., None]), jnp.float32(0.0))
    weight_own = jnp.exp(own_score - peak_score)
    weight_sum = jnp.sum(weight, axis=-1) + weight_own
    rounded = weight.astype(jnp.bfloat16)
    rounded_own = lax.optimization_barrier(weight_own.astype(jnp.bfloat16)).astype(jnp.float32)
    summed = jnp.einsum("sjt,ste->sje", rounded, value_half, preferred_element_type=jnp.float32)
    own_part = rounded_own[..., None] * value_new.astype(jnp.float32)[:, None, :]
    return ((summed + own_part) / weight_sum[..., None]).astype(jnp.bfloat16)


def body(
    queries,
    new_keys,
    new_values,
    cache_keys,
    cache_values,
    lengths,
    parents,
    residual,
    norm_gain,
    vocab_weight,
):
    row_count = lax.axis_size("row")
    beam_count = parents.shape[0]
    slot_cap = max(2, (2 * beam_count + row_count - 1) // row_count)
    group_size = queries.shape[1]
    panel_width = queries.shape[2]
    source = parents // beam_count
    rank_in = count_before(source)
    other_both, other_keys = from_partner(
        (jnp.concatenate([queries, new_keys[:, None, :]], axis=1), cache_keys), "col", 0
    )
    other_queries, other_new_keys = other_both[:, :group_size], other_both[:, group_size]
    offset_part = jnp.broadcast_to(
        (parents % beam_count).astype(jnp.bfloat16)[:, None], (beam_count, panel_width)
    )
    message = jnp.concatenate(
        [
            jnp.concatenate([queries, other_queries], axis=-1),
            jnp.concatenate([new_keys, other_new_keys], axis=-1)[:, None, :],
            jnp.concatenate([new_values, offset_part], axis=-1)[:, None, :],
        ],
        axis=1,
    )
    outgoing = jnp.zeros((row_count, slot_cap) + message.shape[1:], message.dtype)
    outgoing = outgoing.at[source, rank_in].set(message)
    incoming = lax.all_to_all(outgoing, "row", split_axis=0, concat_axis=0, tiled=True)
    incoming = incoming.reshape((row_count * slot_cap,) + message.shape[1:])
    offsets = incoming[:, group_size + 1, panel_width].astype(jnp.int32)
    whole_keys = jnp.concatenate([cache_keys, other_keys], axis=-1)
    served = attend(
        incoming[:, :group_size],
        whole_keys[offsets],
        cache_values[offsets],
        incoming[:, group_size],
        incoming[:, group_size + 1, :panel_width],
        lengths[offsets],
    )
    returned = lax.all_to_all(
        served.reshape((row_count, slot_cap) + served.shape[1:]),
        "row",
        split_axis=0,
        concat_axis=0,
        tiled=True,
    )
    attended = returned[source, rank_in]
    stream = residual.astype(jnp.float32) + attended.astype(jnp.float32)
    square_part = jnp.sum(stream * stream, axis=(1, 2))
    width = group_size * panel_width
    unscaled = (stream * norm_gain.astype(jnp.float32)[None]).astype(jnp.bfloat16)
    extra = jnp.zeros((beam_count, 128), jnp.bfloat16).at[:, :3].set(split_three(square_part))
    packed = jnp.concatenate([unscaled.reshape(beam_count, width), extra], axis=1)
    gathered = gather_from_all(packed, "row")
    flat_rows = gathered[:, :width]
    square_all = jnp.sum(gathered[:, width : width + 3].astype(jnp.float32), axis=1)
    flat_weight = vocab_weight.reshape(width, vocab_weight.shape[2])
    partial = jnp.dot(flat_rows, flat_weight, preferred_element_type=jnp.float32)
    reduced = lax.psum_scatter(partial, "col", scatter_dimension=0, tiled=True)
    col_count = lax.axis_size("col")
    square_parts = lax.all_to_all(
        square_all.reshape(col_count, -1), "col", split_axis=0, concat_axis=0, tiled=True
    )
    scaling = lax.rsqrt(jnp.sum(square_parts, axis=0) / D + 1e-05)
    logits = reduced * scaling[:, None]
    exp_sums = gather_from_all(jnp.sum(jnp.exp(logits), axis=1)[None], "row")
    totals = jnp.sum(exp_sums, axis=0)
    return logits - jnp.log(totals)[:, None]


def solution(mesh):
    placed = (
        P("row", None, "col"),
        P("row", "col"),
        P("row", "col"),
        P("row", None, "col"),
        P("row", None, "col"),
        P("row"),
        P("row"),
        P("row", None, "col"),
        P(None, "col"),
        P(None, "col", "row"),
    )
    return jax.shard_map(
        body, mesh=mesh, in_specs=placed, out_specs=P("col", "row"), check_vma=False
    )
```
